512 devices in a mesh: dp: 4 (over x), shard: 128 (over z, y, core).
Axes of the slice: x: 4, y: 8, z: 8, core: 2. Of those that a mesh axis runs over, the one named last changes fastest.
Arguments:
- grad_parts: float32 [4, 1024, 16384], P('dp', None, 'shard'), may hold values from -0.3 to 0.3
- owner: int32 [1024], replicated, may hold values from 0 to 127, as said below
- master: float32 [4, 128, 4, 128, 128], P('dp', 'shard'), may hold values from -6 to 6
- first_moment: float32 [4, 128, 4, 128, 128], P('dp', 'shard'), may hold values from -0.12 to 0.12
- second_moment: float32 [4, 128, 4, 128, 128], P('dp', 'shard'), may hold values from 0.0001 to 0.001
- left_stat: float32 [4, 128, 4, 128, 128], P('dp', 'shard'), may hold values from -0.0062992126 to 10
- right_stat: float32 [4, 128, 4, 128, 128], P('dp', 'shard'), may hold values from -0.0062992126 to 10
- left_basis: float32 [4, 128, 4, 128, 128], P('dp', 'shard'), may hold values from -0.079549513 to 1.0795495
- right_basis: float32 [4, 128, 4, 128, 128], P('dp', 'shard'), may hold values from -0.079549513 to 1.0795495
Outputs:
- new_params: bfloat16 [1024, 16384], P(None, 'shard')
- master_out: float32 [4, 128, 4, 128, 128], P('dp', 'shard')
- first_out: float32 [4, 128, 4, 128, 128], P('dp', 'shard')
- second_out: float32 [4, 128, 4, 128, 128], P('dp', 'shard')
- left_stat_out: float32 [4, 128, 4, 128, 128], P('dp', 'shard')
- right_stat_out: float32 [4, 128, 4, 128, 128], P('dp', 'shard')
- left_basis_out: float32 [4, 128, 4, 128, 128], P('dp', 'shard')
- right_basis_out: float32 [4, 128, 4, 128, 128], P('dp', 'shard')
The draws below stay inside these ranges and needn't reach their ends.
Inputs may be any that keep to these rules, and one draw needn't show every extreme that they name: In each group of 256 consecutive tiles no owner index holds more than 4 tiles, and some owner holds exactly 4.
All inputs are finite; a program needn't handle non-finite values.
Results may differ from the reference program's by a relative error of at most 0.001.
Values may be sent and summed in bfloat16 or wider, within the bound.
No kernel may reach another device: no remote copies, remote signals or barrier semaphores. Data moves between devices by JAX's collectives and lax.ppermute only.
A program may use at most 64 MiB of HBM per device.

```python
import math
import jax
import jax.numpy as jnp
from jax import lax

B = 128
NS_STEPS = 10
TILES_OWNER = 2
CAP = 4
TG = 256
NT = 1024
N_DP = 4
N_SHARD = 128


def noise_draw(key, shape):
    return jnp.clip(jax.random.normal(key, shape, jnp.float32), -2.5, 2.5) / 2.5


def stat_draw(key):
    shape = (N_DP, N_SHARD, CAP, B, B)
    first_key, second_key = jax.random.split(key)
    diag_values = jnp.exp(jax.random.uniform(first_key, shape[:-1], jnp.float32, 0.0, math.log(10.0)))
    eye_mask = jnp.eye(B, dtype=jnp.float32)
    noise = noise_draw(second_key, shape)
    return eye_mask * diag_values[..., None] + (1.0 - eye_mask) * noise * (0.8 / (B - 1))


def basis_draw(key):
    shape = (N_DP, N_SHARD, CAP, B, B)
    eye_mask = jnp.eye(B, dtype=jnp.float32)
    return eye_mask + noise_draw(key, shape) * (0.9 / math.sqrt(B))


def draw_left_stat(key, part):
    return stat_draw(jax.random.fold_in(key, 101))


def draw_right_stat(key, part):
    return stat_draw(jax.random.fold_in(key, 202))


def draw_left_basis(key, part):
    return basis_draw(jax.random.fold_in(key, 303))


def draw_right_basis(key, part):
    return basis_draw(jax.random.fold_in(key, 404))


def owner_group(key):
    first_key, second_key, third_key = jax.random.split(key, 3)
    quarter = N_SHARD // 4
    offsets = jax.random.randint(first_key, (quarter,), -1, 2).astype(jnp.int32)
    counts = jnp.concatenate([jnp.full((quarter,), CAP, jnp.int32), jnp.zeros((quarter,), jnp.int32), TILES_OWNER + offsets, TILES_OWNER - offsets])
    order = jax.random.permutation(second_key, N_SHARD)
    by_owner = jnp.zeros((N_SHARD,), jnp.int32).at[order].set(counts)
    listed = jnp.repeat(jnp.arange(N_SHARD, dtype=jnp.int32), by_owner, total_repeat_length=TG)
    return jax.random.permutation(third_key, listed)


def draw_owner(key, part):
    group_keys = jax.random.split(jax.random.fold_in(key, 505), N_DP)
    return jax.vmap(owner_group)(group_keys).reshape(-1).astype(jnp.int32)


def with_spikes(drawn, stream_key, source, target, parts, factor):
    def block_of(axis_at):
        return (jnp.arange(drawn.shape[axis_at]) // (drawn.shape[axis_at] // parts)).reshape((-1,) + (1,) * (drawn.ndim - 1 - axis_at))

    near = jax.random.permutation(stream_key, parts)[block_of(target)]
    second = (block_of(target) + parts // 2) % parts
    return jnp.where((block_of(source) == near) | (block_of(source) == second), factor * drawn, drawn)


def steps_of(key, extent, cuts, low, high):
    gain = 1.0
    for axis_at, shards_of in cuts:
        draws = jax.random.uniform(jax.random.fold_in(jax.random.fold_in(key, 6), axis_at), (shards_of,), jnp.float32, low / len(cuts), high / len(cuts))
        gain = gain * jnp.repeat(jnp.exp(draws), extent[axis_at] // shards_of).reshape((-1,) + (1,) * (len(extent) - 1 - axis_at))
    return gain


def scatter_about(key, shape, scale, bound, pieces=(), kind=jnp.bfloat16):
    values = jax.random.normal(key, shape, jnp.float32) * scale
    if len(pieces) > 0:
        values = steps_of(key, shape, pieces, -0.22, 0.18) * values
    return jnp.clip(values, min=-bound, max=bound).astype(kind)


def gaussian_with(key, shape, deviation, most, cuts, heavy, kind=jnp.bfloat16):
    values = deviation * jax.random.normal(key, shape, jnp.float32)
    if cuts:
        values = values * steps_of(key, shape, cuts, -0.22, 0.18)
    return jnp.clip(with_spikes(values, jax.random.fold_in(key, 3), *heavy), -most, most).astype(kind)


def setup_inputs(seed: int = 0) -> dict:
    streams_of = jax.random.split(jax.random.key(seed), 10)
    return {
        "grad_parts": gaussian_with(streams_of[0], (N_DP, NT, B * B), 0.05, 0.3, ((0, 4), (2, 128)), (0, 1, 4, 2.0), jnp.float32),
        "owner": draw_owner(jax.random.fold_in(streams_of[9], 71), 0),
        "master": scatter_about(streams_of[2], (N_DP, N_SHARD, CAP, B, B), 1.0, 6.0, ((0, 4), (1, 128)), jnp.float32),
        "first_moment": scatter_about(streams_of[3], (N_DP, N_SHARD, CAP, B, B), 0.02, 0.12, ((0, 4), (1, 128)), jnp.float32),
        "second_moment": jnp.clip(jnp.exp(math.log(0.001) - 2.3025852 * jax.random.uniform(streams_of[4], (N_DP, N_SHARD, CAP, B, B), jnp.float32) ** steps_of(streams_of[4], (N_DP, N_SHARD, CAP, B, B), ((0, 4), (1, 128)), -0.2, 0.2)), 0.0001, 0.001),
        "left_stat": draw_left_stat(jax.random.fold_in(streams_of[9], 71), 0),
        "right_stat": draw_right_stat(jax.random.fold_in(streams_of[9], 71), 0),
        "left_basis": draw_left_basis(jax.random.fold_in(streams_of[9], 71), 0),
        "right_basis": draw_right_basis(jax.random.fold_in(streams_of[9], 71), 0),
    }


beta_one = 0.9
beta_two = 0.95
stat_decay = 0.95
learn_rate = 0.05
weight_decay = 0.01
adam_eps = 1e-08
highest = lax.Precision.HIGHEST

def product(form, left, right):
    return jnp.einsum(form, left, right, precision=highest)

def slot_index(owners, shards):
    matches = (owners[..., None] == jnp.arange(shards, dtype=jnp.int32)).astype(jnp.int32)
    running = jnp.cumsum(matches, axis=1)
    return (lax.optimization_barrier(jnp.sum(matches * running, axis=-1)) - 1).astype(jnp.int32)

def orthogonal(pending):
    iterate = pending * lax.rsqrt(lax.optimization_barrier(jnp.sum(pending * pending, axis=(1, 2), keepdims=True)) + 1e-06)
    for step in range(NS_STEPS):
        gram = product('nik,njk->nij', iterate, iterate)
        iterate = 1.5 * iterate - 0.5 * product('nij,njk->nik', gram, iterate)
    return iterate

def soap_update(gradient, master, first, second, lstat, rstat, lbasis, rbasis):
    first_new = beta_one * first + (1.0 - beta_one) * gradient
    grad_rot = product('nik,nkl->nil', product('nji,njk->nik', lbasis, gradient), rbasis)
    first_rot = product('nik,nkl->nil', product('nji,njk->nik', lbasis, first_new), rbasis)
    second_new = beta_two * second + (1.0 - beta_two) * grad_rot * grad_rot
    normed = first_rot / (jnp.sqrt(second_new) + adam_eps)
    update = product('nik,nlk->nil', product('nij,njk->nik', lbasis, normed), rbasis)
    master_new = master - learn_rate * (update + weight_decay * master)
    lstat_new = stat_decay * lstat + (1.0 - stat_decay) * product('nik,njk->nij', gradient, gradient)
    rstat_new = stat_decay * rstat + (1.0 - stat_decay) * product('nki,nkj->nij', gradient, gradient)
    lbasis_new = orthogonal(product('nij,njk->nik', lstat_new, lbasis))
    rbasis_new = orthogonal(product('nij,njk->nik', rstat_new, rbasis))
    return (master_new, first_new, second_new, lstat_new, rstat_new, lbasis_new, rbasis_new)

def reference(grad_parts, owner, master, first_moment, second_moment, left_stat, right_stat, left_basis, right_basis):
    summed = lax.optimization_barrier(jnp.sum(grad_parts, axis=0))
    owners = owner.reshape(N_DP, TG)
    place_index = (owners * CAP + slot_index(owners, N_SHARD)).astype(jnp.int32)
    group_ids = jnp.broadcast_to(jnp.arange(N_DP, dtype=jnp.int32)[:, None], (N_DP, TG))
    slot_grad = jnp.zeros((N_DP, N_SHARD * CAP, B, B), jnp.float32)
    slot_grad = slot_grad.at[group_ids, place_index].set(summed.reshape(N_DP, TG, B, B))
    count = N_DP * N_SHARD * CAP

    def flatten(array):
        return array.reshape(count, B, B)
    results = soap_update(flatten(slot_grad), flatten(master), flatten(first_moment), flatten(second_moment), flatten(left_stat), flatten(right_stat), flatten(left_basis), flatten(right_basis))
    shaped = [item.reshape(N_DP, N_SHARD, CAP, B, B) for item in results]
    picked = shaped[0].reshape(N_DP, N_SHARD * CAP, B, B)[group_ids, place_index]
    new_params = picked.reshape(NT, B * B).astype(jnp.bfloat16)
    return (new_params, shaped[0], shaped[1], shaped[2], shaped[3], shaped[4], shaped[5], shaped[6])
```

```python
import jax
import jax.numpy as jnp
from jax import lax
from jax.sharding import PartitionSpec as P

NS_STEPS = 10


beta_one = 0.9
beta_two = 0.95
stat_decay = 0.95
learn_rate = 0.05
weight_decay = 0.01
adam_eps = 1e-08
highest = lax.Precision.HIGHEST


def product(form, left, right):
    return jnp.einsum(form, left, right, precision=highest)


def slot_index(owners, shards):
    matches = (owners[..., None] == jnp.arange(shards, dtype=jnp.int32)).astype(jnp.int32)
    running = jnp.cumsum(matches, axis=1)
    return jnp.sum(matches * running, axis=-1) - 1


def orthogonal(pending):
    iterate = pending * lax.rsqrt(jnp.sum(pending * pending, axis=(1, 2), keepdims=True) + 1e-06)
    for step in range(NS_STEPS):
        gram = product("nik,njk->nij", iterate, iterate)
        iterate = 1.5 * iterate - 0.5 * product("nij,njk->nik", gram, iterate)
    return iterate


def soap_weights(gradient, master, first, second, lbasis, rbasis):
    count = gradient.shape[0]
    first_new = beta_one * first + (1.0 - beta_one) * gradient
    both = jnp.concatenate([gradient, first_new], axis=0)
    lboth = jnp.concatenate([lbasis, lbasis], axis=0)
    rboth = jnp.concatenate([rbasis, rbasis], axis=0)
    rotated = product("nik,nkl->nil", product("nji,njk->nik", lboth, both), rboth)
    grad_rot, first_rot = rotated[:count], rotated[count:]
    second_new = beta_two * second + (1.0 - beta_two) * grad_rot * grad_rot
    normed = first_rot / (jnp.sqrt(second_new) + adam_eps)
    update = product("nik,nlk->nil", product("nij,njk->nik", lbasis, normed), rbasis)
    master_new = master - learn_rate * (update + weight_decay * master)
    return master_new, first_new, second_new


def soap_bases(gradient, lstat, rstat, lbasis, rbasis):
    count = gradient.shape[0]
    lstat_new = stat_decay * lstat + (1.0 - stat_decay) * product(
        "nik,njk->nij", gradient, gradient
    )
    rstat_new = stat_decay * rstat + (1.0 - stat_decay) * product(
        "nki,nkj->nij", gradient, gradient
    )
    pending = product(
        "nij,njk->nik",
        jnp.concatenate([lstat_new, rstat_new], axis=0),
        jnp.concatenate([lbasis, rbasis], axis=0),
    )
    bases = orthogonal(pending)
    return lstat_new, rstat_new, bases[:count], bases[count:]


def body(
    grad_parts,
    owner,
    master,
    first_moment,
    second_moment,
    left_stat,
    right_stat,
    left_basis,
    right_basis,
):
    shards = lax.axis_size("shard")
    groups = lax.axis_size("dp")
    my_group = lax.axis_index("dp")
    capacity = master.shape[2]
    block_size = master.shape[4]
    piece_len = grad_parts.shape[2]
    tile_count = owner.shape[0]
    per_group = tile_count // groups
    owners = owner.reshape(groups, per_group)
    place_index = slot_index(owners, shards) * shards + owners
    own_place = lax.dynamic_index_in_dim(place_index, my_group, 0, keepdims=False)
    parts = grad_parts.reshape(groups, per_group, piece_len)
    summed = jnp.sum(lax.all_to_all(parts, "dp", 0, 0, tiled=True), axis=0)
    outgoing = jnp.zeros((capacity * shards, piece_len), jnp.float32)
    outgoing = outgoing.at[own_place].set(summed)
    outgoing = outgoing.reshape(capacity, shards, piece_len)
    incoming = lax.all_to_all(outgoing, "shard", split_axis=1, concat_axis=1, tiled=True)

    def as_tiles(array):
        return array.reshape(capacity, block_size, block_size)

    gradient = incoming.reshape(capacity, block_size, block_size)
    master_new, first_new, second_new = soap_weights(
        gradient,
        as_tiles(master),
        as_tiles(first_moment),
        as_tiles(second_moment),
        as_tiles(left_basis),
        as_tiles(right_basis),
    )
    weights = master_new.astype(jnp.bfloat16)
    weights, gradient, left_stat, right_stat, left_basis, right_basis = lax.optimization_barrier(
        (weights, gradient, left_stat, right_stat, left_basis, right_basis)
    )
    returned = lax.all_to_all(weights, "shard", split_axis=1, concat_axis=1, tiled=True)
    returned = returned.reshape(capacity * shards, piece_len)
    own_rows = returned[own_place]
    spread = jnp.broadcast_to(own_rows[None], (groups,) + own_rows.shape)
    new_params = lax.all_to_all(spread, "dp", 0, 0, tiled=True).reshape(tile_count, piece_len)
    lstat_new, rstat_new, lbasis_new, rbasis_new = soap_bases(
        gradient,
        as_tiles(left_stat),
        as_tiles(right_stat),
        as_tiles(left_basis),
        as_tiles(right_basis),
    )
    results = (master_new, first_new, second_new, lstat_new, rstat_new, lbasis_new, rbasis_new)
    shaped = [item.reshape(1, 1, capacity, block_size, block_size) for item in results]
    return (new_params, *shaped)


def solution(mesh):
    state = P("dp", "shard", None, None, None)
    placed = (P("dp", None, "shard"), P()) + (state,) * 7
    return jax.shard_map(
        body,
        mesh=mesh,
        in_specs=placed,
        out_specs=(P(None, "shard"),) + (state,) * 7,
        check_vma=False,
    )
```

```python
import jax
import jax.numpy as jnp
from jax import lax
from jax.sharding import PartitionSpec as P

NS_STEPS = 10


beta_one = 0.9
beta_two = 0.95
stat_decay = 0.95
learn_rate = 0.05
weight_decay = 0.01
adam_eps = 1e-08
highest = lax.Precision.HIGHEST
high = lax.Precision.HIGH


def product(form, left, right, precision=highest):
    return jnp.einsum(form, left, right, precision=precision)


def slot_index(owners, shards):
    matches = (owners[..., None] == jnp.arange(shards, dtype=jnp.int32)).astype(jnp.int32)
    running = jnp.cumsum(matches, axis=1)
    return jnp.sum(matches * running, axis=-1) - 1


def orthogonal(pending):
    iterate = pending * lax.rsqrt(jnp.sum(pending * pending, axis=(1, 2), keepdims=True) + 1e-06)
    for step in range(NS_STEPS):
        gram = product("nik,njk->nij", iterate, iterate, high)
        iterate = 1.5 * iterate - 0.5 * product("nij,njk->nik", gram, iterate, high)
    return iterate


def soap_weights(gradient, master, first, second, lbasis, rbasis):
    count = gradient.shape[0]
    first_new = beta_one * first + (1.0 - beta_one) * gradient
    both = jnp.concatenate([gradient, first_new], axis=0)
    lboth = jnp.concatenate([lbasis, lbasis], axis=0)
    rboth = jnp.concatenate([rbasis, rbasis], axis=0)
    rotated = product("nik,nkl->nil", product("nji,njk->nik", lboth, both), rboth)
    grad_rot, first_rot = rotated[:count], rotated[count:]
    second_new = beta_two * second + (1.0 - beta_two) * grad_rot * grad_rot
    normed = first_rot / (jnp.sqrt(second_new) + adam_eps)
    update = product("nik,nlk->nil", product("nij,njk->nik", lbasis, normed), rbasis)
    master_new = master - learn_rate * (update + weight_decay * master)
    return master_new, first_new, second_new


def soap_bases(gradient, lstat, rstat, lbasis, rbasis):
    count = gradient.shape[0]
    lstat_new = stat_decay * lstat + (1.0 - stat_decay) * product(
        "nik,njk->nij", gradient, gradient
    )
    rstat_new = stat_decay * rstat + (1.0 - stat_decay) * product(
        "nki,nkj->nij", gradient, gradient
    )
    pending = product(
        "nij,njk->nik",
        jnp.concatenate([lstat_new, rstat_new], axis=0),
        jnp.concatenate([lbasis, rbasis], axis=0),
    )
    bases = orthogonal(pending)
    return lstat_new, rstat_new, bases[:count], bases[count:]


def body(
    grad_parts,
    owner,
    master,
    first_moment,
    second_moment,
    left_stat,
    right_stat,
    left_basis,
    right_basis,
):
    shards = lax.axis_size("shard")
    groups = lax.axis_size("dp")
    my_group = lax.axis_index("dp")
    capacity = master.shape[2]
    block_size = master.shape[4]
    piece_len = grad_parts.shape[2]
    tile_count = owner.shape[0]
    per_group = tile_count // groups
    owners = owner.reshape(groups, per_group)
    place_index = slot_index(owners, shards) * shards + owners
    own_place = lax.dynamic_index_in_dim(place_index, my_group, 0, keepdims=False)
    parts = grad_parts.reshape(groups, per_group, piece_len)
    summed = jnp.sum(lax.all_to_all(parts, "dp", 0, 0, tiled=True), axis=0)
    outgoing = jnp.zeros((capacity * shards, piece_len), jnp.float32)
    outgoing = outgoing.at[own_place].set(summed)
    outgoing = outgoing.reshape(capacity, shards, piece_len)
    incoming = lax.all_to_all(outgoing, "shard", split_axis=1, concat_axis=1, tiled=True)

    def as_tiles(array):
        return array.reshape(capacity, block_size, block_size)

    gradient = incoming.reshape(capacity, block_size, block_size)
    master_new, first_new, second_new = soap_weights(
        gradient,
        as_tiles(master),
        as_tiles(first_moment),
        as_tiles(second_moment),
        as_tiles(left_basis),
        as_tiles(right_basis),
    )
    weights = master_new.astype(jnp.bfloat16)
    weights, gradient, left_stat, right_stat, left_basis, right_basis = lax.optimization_barrier(
        (weights, gradient, left_stat, right_stat, left_basis, right_basis)
    )
    returned = lax.all_to_all(weights, "shard", split_axis=1, concat_axis=1, tiled=True)
    returned = returned.reshape(capacity * shards, piece_len)
    own_rows = returned[own_place]
    spread = jnp.broadcast_to(own_rows[None], (groups,) + own_rows.shape)
    new_params = lax.all_to_all(spread, "dp", 0, 0, tiled=True).reshape(tile_count, piece_len)
    lstat_new, rstat_new, lbasis_new, rbasis_new = soap_bases(
        gradient,
        as_tiles(left_stat),
        as_tiles(right_stat),
        as_tiles(left_basis),
        as_tiles(right_basis),
    )
    results = (master_new, first_new, second_new, lstat_new, rstat_new, lbasis_new, rbasis_new)
    shaped = [item.reshape(1, 1, capacity, block_size, block_size) for item in results]
    return (new_params, *shaped)


def solution(mesh):
    state = P("dp", "shard", None, None, None)
    placed = (P("dp", None, "shard"), P()) + (state,) * 7
    return jax.shard_map(
        body,
        mesh=mesh,
        in_specs=placed,
        out_specs=(P(None, "shard"),) + (state,) * 7,
        check_vma=False,
    )
```

```python
import jax
import jax.numpy as jnp
from jax import lax
from jax.sharding import PartitionSpec as P

NS_STEPS = 10


beta_one = 0.9
beta_two = 0.95
stat_decay = 0.95
learn_rate = 0.05
weight_decay = 0.01
adam_eps = 1e-08
highest = lax.Precision.HIGHEST
high = lax.Precision.HIGH


def product(form, left, right, precision=highest):
    return jnp.einsum(form, left, right, precision=precision)


def slot_index(owners, shards):
    matches = (owners[..., None] == jnp.arange(shards, dtype=jnp.int32)).astype(jnp.int32)
    running = jnp.cumsum(matches, axis=1)
    return jnp.sum(matches * running, axis=-1) - 1


def orthogonal(pending):
    iterate = pending * lax.rsqrt(jnp.sum(pending * pending, axis=(1, 2), keepdims=True) + 1e-06)
    def newton_schulz(step, iterate):
        gram = product("nik,njk->nij", iterate, iterate, high)
        return 1.5 * iterate - 0.5 * product("nij,njk->nik", gram, iterate, high)

    return lax.fori_loop(0, NS_STEPS, newton_schulz, iterate)


def soap_weights(gradient, master, first, second, lbasis, rbasis):
    count = gradient.shape[0]
    first_new = beta_one * first + (1.0 - beta_one) * gradient
    both = jnp.concatenate([gradient, first_new], axis=0)
    lboth = jnp.concatenate([lbasis, lbasis], axis=0)
    rboth = jnp.concatenate([rbasis, rbasis], axis=0)
    rotated = product("nik,nkl->nil", product("nji,njk->nik", lboth, both), rboth)
    grad_rot, first_rot = rotated[:count], rotated[count:]
    second_new = beta_two * second + (1.0 - beta_two) * grad_rot * grad_rot
    normed = first_rot / (jnp.sqrt(second_new) + adam_eps)
    update = product("nik,nlk->nil", product("nij,njk->nik", lbasis, normed), rbasis)
    master_new = master - learn_rate * (update + weight_decay * master)
    return master_new, first_new, second_new


def soap_bases(gradient, lstat, rstat, lbasis, rbasis):
    count = gradient.shape[0]
    lstat_new = stat_decay * lstat + (1.0 - stat_decay) * product(
        "nik,njk->nij", gradient, gradient
    )
    rstat_new = stat_decay * rstat + (1.0 - stat_decay) * product(
        "nki,nkj->nij", gradient, gradient
    )
    pending = product(
        "nij,njk->nik",
        jnp.concatenate([lstat_new, rstat_new], axis=0),
        jnp.concatenate([lbasis, rbasis], axis=0),
    )
    bases = orthogonal(pending)
    return lstat_new, rstat_new, bases[:count], bases[count:]


def body(
    grad_parts,
    owner,
    master,
    first_moment,
    second_moment,
    left_stat,
    right_stat,
    left_basis,
    right_basis,
):
    shards = lax.axis_size("shard")
    groups = lax.axis_size("dp")
    my_group = lax.axis_index("dp")
    capacity = master.shape[2]
    block_size = master.shape[4]
    piece_len = grad_parts.shape[2]
    tile_count = owner.shape[0]
    per_group = tile_count // groups
    owners = owner.reshape(groups, per_group)
    place_index = slot_index(owners, shards) * shards + owners
    own_place = lax.dynamic_index_in_dim(place_index, my_group, 0, keepdims=False)
    parts = grad_parts.reshape(groups, per_group, piece_len)
    summed = jnp.sum(lax.all_to_all(parts, "dp", 0, 0, tiled=True), axis=0)
    outgoing = jnp.zeros((capacity * shards, piece_len), jnp.float32)
    outgoing = outgoing.at[own_place].set(summed)
    outgoing = outgoing.reshape(capacity, shards, piece_len)
    incoming = lax.all_to_all(outgoing, "shard", split_axis=1, concat_axis=1, tiled=True)

    def as_tiles(array):
        return array.reshape(capacity, block_size, block_size)

    gradient = incoming.reshape(capacity, block_size, block_size)
    master_new, first_new, second_new = soap_weights(
        gradient,
        as_tiles(master),
        as_tiles(first_moment),
        as_tiles(second_moment),
        as_tiles(left_basis),
        as_tiles(right_basis),
    )
    weights = master_new.astype(jnp.bfloat16)
    weights, gradient, left_stat, right_stat, left_basis, right_basis = lax.optimization_barrier(
        (weights, gradient, left_stat, right_stat, left_basis, right_basis)
    )
    returned = lax.all_to_all(weights, "shard", split_axis=1, concat_axis=1, tiled=True)
    returned = returned.reshape(capacity * shards, piece_len)
    own_rows = returned[own_place]
    spread = jnp.broadcast_to(own_rows[None], (groups,) + own_rows.shape)
    new_params = lax.all_to_all(spread, "dp", 0, 0, tiled=True).reshape(tile_count, piece_len)
    lstat_new, rstat_new, lbasis_new, rbasis_new = soap_bases(
        gradient,
        as_tiles(left_stat),
        as_tiles(right_stat),
        as_tiles(left_basis),
        as_tiles(right_basis),
    )
    results = (master_new, first_new, second_new, lstat_new, rstat_new, lbasis_new, rbasis_new)
    shaped = [item.reshape(1, 1, capacity, block_size, block_size) for item in results]
    return (new_params, *shaped)


def solution(mesh):
    state = P("dp", "shard", None, None, None)
    placed = (P("dp", None, "shard"), P()) + (state,) * 7
    return jax.shard_map(
        body,
        mesh=mesh,
        in_specs=placed,
        out_specs=(P(None, "shard"),) + (state,) * 7,
        check_vma=False,
    )
```

```python
import jax
import jax.numpy as jnp
from jax import lax
from jax.sharding import PartitionSpec as P

NS_STEPS = 10


beta_one = 0.9
beta_two = 0.95
stat_decay = 0.95
learn_rate = 0.05
weight_decay = 0.01
adam_eps = 1e-08
highest = lax.Precision.HIGHEST
high = lax.Precision.HIGH


def product(form, left, right, precision=high):
    return jnp.einsum(form, left, right, precision=precision)


def slot_index(owners, shards):
    matches = (owners[..., None] == jnp.arange(shards, dtype=jnp.int32)).astype(jnp.int32)
    running = jnp.cumsum(matches, axis=1)
    return jnp.sum(matches * running, axis=-1) - 1


def orthogonal(pending):
    iterate = pending * lax.rsqrt(jnp.sum(pending * pending, axis=(1, 2), keepdims=True) + 1e-06)
    def newton_schulz(step, iterate):
        gram = product("nik,njk->nij", iterate, iterate, high)
        return 1.5 * iterate - 0.5 * product("nij,njk->nik", gram, iterate, high)

    return lax.fori_loop(0, NS_STEPS, newton_schulz, iterate)


def soap_weights(gradient, master, first, second, lbasis, rbasis):
    count = gradient.shape[0]
    first_new = beta_one * first + (1.0 - beta_one) * gradient
    both = jnp.concatenate([gradient, first_new], axis=0)
    lboth = jnp.concatenate([lbasis, lbasis], axis=0)
    rboth = jnp.concatenate([rbasis, rbasis], axis=0)
    rotated = product("nik,nkl->nil", product("nji,njk->nik", lboth, both), rboth)
    grad_rot, first_rot = rotated[:count], rotated[count:]
    second_new = beta_two * second + (1.0 - beta_two) * grad_rot * grad_rot
    normed = first_rot / (jnp.sqrt(second_new) + adam_eps)
    update = product("nik,nlk->nil", product("nij,njk->nik", lbasis, normed), rbasis)
    master_new = master - learn_rate * (update + weight_decay * master)
    return master_new, first_new, second_new


def soap_bases(gradient, lstat, rstat, lbasis, rbasis):
    count = gradient.shape[0]
    lstat_new = stat_decay * lstat + (1.0 - stat_decay) * product(
        "nik,njk->nij", gradient, gradient
    )
    rstat_new = stat_decay * rstat + (1.0 - stat_decay) * product(
        "nki,nkj->nij", gradient, gradient
    )
    pending = product(
        "nij,njk->nik",
        jnp.concatenate([lstat_new, rstat_new], axis=0),
        jnp.concatenate([lbasis, rbasis], axis=0),
    )
    bases = orthogonal(pending)
    return lstat_new, rstat_new, bases[:count], bases[count:]


def body(
    grad_parts,
    owner,
    master,
    first_moment,
    second_moment,
    left_stat,
    right_stat,
    left_basis,
    right_basis,
):
    shards = lax.axis_size("shard")
    groups = lax.axis_size("dp")
    my_group = lax.axis_index("dp")
    capacity = master.shape[2]
    block_size = master.shape[4]
    piece_len = grad_parts.shape[2]
    tile_count = owner.shape[0]
    per_group = tile_count // groups
    owners = owner.reshape(groups, per_group)
    place_index = slot_index(owners, shards) * shards + owners
    own_place = lax.dynamic_index_in_dim(place_index, my_group, 0, keepdims=False)
    parts = grad_parts.reshape(groups, per_group, piece_len)
    summed = jnp.sum(lax.all_to_all(parts, "dp", 0, 0, tiled=True), axis=0)
    outgoing = jnp.zeros((capacity * shards, piece_len), jnp.float32)
    outgoing = outgoing.at[own_place].set(summed)
    outgoing = outgoing.reshape(capacity, shards, piece_len)
    incoming = lax.all_to_all(outgoing, "shard", split_axis=1, concat_axis=1, tiled=True)

    def as_tiles(array):
        return array.reshape(capacity, block_size, block_size)

    gradient = incoming.reshape(capacity, block_size, block_size)
    master_new, first_new, second_new = soap_weights(
        gradient,
        as_tiles(master),
        as_tiles(first_moment),
        as_tiles(second_moment),
        as_tiles(left_basis),
        as_tiles(right_basis),
    )
    weights = master_new.astype(jnp.bfloat16)
    returned = lax.all_to_all(weights, "shard", split_axis=1, concat_axis=1, tiled=True)
    returned = returned.reshape(capacity * shards, piece_len)
    own_rows = returned[own_place]
    spread = jnp.broadcast_to(own_rows[None], (groups,) + own_rows.shape)
    new_params = lax.all_to_all(spread, "dp", 0, 0, tiled=True).reshape(tile_count, piece_len)
    lstat_new, rstat_new, lbasis_new, rbasis_new = soap_bases(
        gradient,
        as_tiles(left_stat),
        as_tiles(right_stat),
        as_tiles(left_basis),
        as_tiles(right_basis),
    )
    results = (master_new, first_new, second_new, lstat_new, rstat_new, lbasis_new, rbasis_new)
    shaped = [item.reshape(1, 1, capacity, block_size, block_size) for item in results]
    return (new_params, *shaped)


def solution(mesh):
    state = P("dp", "shard", None, None, None)
    placed = (P("dp", None, "shard"), P()) + (state,) * 7
    return jax.shard_map(
        body,
        mesh=mesh,
        in_specs=placed,
        out_specs=(P(None, "shard"),) + (state,) * 7,
        check_vma=False,
    )
```

```python
import jax
import jax.numpy as jnp
from jax import lax
from jax.sharding import PartitionSpec as P

NS_STEPS = 10


beta_one = 0.9
beta_two = 0.95
stat_decay = 0.95
learn_rate = 0.05
weight_decay = 0.01
adam_eps = 1e-08
highest = lax.Precision.HIGHEST
high = lax.Precision.HIGH


def product(form, left, right, precision=high):
    return jnp.einsum(form, left, right, precision=precision)


def slot_index(owners, shards):
    matches = (owners[..., None] == jnp.arange(shards, dtype=jnp.int32)).astype(jnp.int32)
    running = jnp.cumsum(matches, axis=1)
    return jnp.sum(matches * running, axis=-1) - 1


def orthogonal(pending):
    iterate = pending * lax.rsqrt(jnp.sum(pending * pending, axis=(1, 2), keepdims=True) + 1e-06)
    def newton_schulz(step, iterate):
        gram = product("nik,njk->nij", iterate, iterate, high)
        return 1.5 * iterate - 0.5 * product("nij,njk->nik", gram, iterate, high)

    return lax.fori_loop(0, NS_STEPS, newton_schulz, iterate)


def soap_weights(gradient, master, first, second, lbasis, rbasis):
    count = gradient.shape[0]
    first_new = beta_one * first + (1.0 - beta_one) * gradient
    both = jnp.concatenate([gradient, first_new], axis=0)
    lboth = jnp.concatenate([lbasis, lbasis], axis=0)
    rboth = jnp.concatenate([rbasis, rbasis], axis=0)
    rotated = product("nik,nkl->nil", product("nji,njk->nik", lboth, both), rboth)
    grad_rot, first_rot = rotated[:count], rotated[count:]
    second_new = beta_two * second + (1.0 - beta_two) * grad_rot * grad_rot
    normed = first_rot / (jnp.sqrt(second_new) + adam_eps)
    update = product("nik,nlk->nil", product("nij,njk->nik", lbasis, normed), rbasis)
    master_new = master - learn_rate * (update + weight_decay * master)
    return master_new, first_new, second_new


def soap_bases(gradient, lstat, rstat, lbasis, rbasis):
    count = gradient.shape[0]
    lstat_new = stat_decay * lstat + (1.0 - stat_decay) * product(
        "nik,njk->nij", gradient, gradient
    )
    rstat_new = stat_decay * rstat + (1.0 - stat_decay) * product(
        "nki,nkj->nij", gradient, gradient
    )
    pending = product(
        "nij,njk->nik",
        jnp.concatenate([lstat_new, rstat_new], axis=0),
        jnp.concatenate([lbasis, rbasis], axis=0),
    )
    bases = orthogonal(pending)
    return lstat_new, rstat_new, bases[:count], bases[count:]


def body(
    grad_parts,
    owner,
    master,
    first_moment,
    second_moment,
    left_stat,
    right_stat,
    left_basis,
    right_basis,
):
    shards = lax.axis_size("shard")
    groups = lax.axis_size("dp")
    my_group = lax.axis_index("dp")
    capacity = master.shape[2]
    block_size = master.shape[4]
    piece_len = grad_parts.shape[2]
    tile_count = owner.shape[0]
    per_group = tile_count // groups
    owners = owner.reshape(groups, per_group)
    place_index = owners * capacity + slot_index(owners, shards)
    own_place = lax.dynamic_index_in_dim(place_index, my_group, 0, keepdims=False)
    parts = grad_parts.reshape(groups, per_group, piece_len)
    summed = jnp.sum(lax.all_to_all(parts, "dp", 0, 0, tiled=True), axis=0)
    places = jnp.arange(capacity * shards, dtype=jnp.int32)
    placing = (places[:, None] == own_place[None, :]).astype(jnp.float32)
    outgoing = jnp.dot(placing, summed, precision=highest)
    outgoing = outgoing.reshape(shards, capacity, piece_len).transpose(1, 0, 2)
    incoming = lax.all_to_all(outgoing, "shard", split_axis=1, concat_axis=1, tiled=True)

    def as_tiles(array):
        return array.reshape(capacity, block_size, block_size)

    gradient = incoming.reshape(capacity, block_size, block_size)
    master_new, first_new, second_new = soap_weights(
        gradient,
        as_tiles(master),
        as_tiles(first_moment),
        as_tiles(second_moment),
        as_tiles(left_basis),
        as_tiles(right_basis),
    )
    weights = master_new.astype(jnp.bfloat16)
    weights = weights.transpose(1, 0, 2)
    returned = lax.all_to_all(weights, "shard", split_axis=0, concat_axis=0, tiled=True)
    returned = returned.reshape(shards * capacity, piece_len)
    picking = (own_place[:, None] == places[None, :]).astype(jnp.bfloat16)
    picking = jnp.broadcast_to(picking[None], (groups,) + picking.shape)
    spread = jnp.einsum("gtp,pc->gtc", picking, returned, preferred_element_type=jnp.float32)
    spread = spread.astype(jnp.bfloat16)
    new_params = lax.all_to_all(spread, "dp", 0, 0, tiled=True).reshape(tile_count, piece_len)
    lstat_new, rstat_new, lbasis_new, rbasis_new = soap_bases(
        gradient,
        as_tiles(left_stat),
        as_tiles(right_stat),
        as_tiles(left_basis),
        as_tiles(right_basis),
    )
    results = (master_new, first_new, second_new, lstat_new, rstat_new, lbasis_new, rbasis_new)
    shaped = [item.reshape(1, 1, capacity, block_size, block_size) for item in results]
    return (new_params, *shaped)


def solution(mesh):
    state = P("dp", "shard", None, None, None)
    placed = (P("dp", None, "shard"), P()) + (state,) * 7
    return jax.shard_map(
        body,
        mesh=mesh,
        in_specs=placed,
        out_specs=(P(None, "shard"),) + (state,) * 7,
        check_vma=False,
    )
```

```python
import jax
import jax.numpy as jnp
from jax import lax
from jax.sharding import PartitionSpec as P

NS_STEPS = 10


beta_one = 0.9
beta_two = 0.95
stat_decay = 0.95
learn_rate = 0.05
weight_decay = 0.01
adam_eps = 1e-08
highest = lax.Precision.HIGHEST
high = lax.Precision.HIGH


def product(form, left, right, precision=high):
    return jnp.einsum(form, left, right, precision=precision)


def slot_index(owners, shards):
    matches = (owners[..., None] == jnp.arange(shards, dtype=jnp.int32)).astype(jnp.int32)
    running = jnp.cumsum(matches, axis=1)
    return jnp.sum(matches * running, axis=-1) - 1


def orthogonal(pending):
    iterate = pending * lax.rsqrt(jnp.sum(pending * pending, axis=(1, 2), keepdims=True) + 1e-06)
    def newton_schulz(step, iterate):
        gram = product("nik,njk->nij", iterate, iterate, high)
        return 1.5 * iterate - 0.5 * product("nij,njk->nik", gram, iterate, high)

    return lax.fori_loop(0, NS_STEPS, newton_schulz, iterate)


def rotate(lbasis, tiles, rbasis):
    return product("nik,nkl->nil", product("nji,njk->nik", lbasis, tiles), rbasis)


def soap_weights(gradient, first, second, lbasis, rbasis, first_held, master_held):
    first_new = beta_one * first + (1.0 - beta_one) * gradient
    grad_rot = rotate(lbasis, gradient, rbasis)
    first_rot = beta_one * first_held + (1.0 - beta_one) * grad_rot
    second_new = beta_two * second + (1.0 - beta_two) * grad_rot * grad_rot
    normed = first_rot / (jnp.sqrt(second_new) + adam_eps)
    update = product("nik,nlk->nil", product("nij,njk->nik", lbasis, normed), rbasis)
    master_new = master_held - learn_rate * update
    return master_new, first_new, second_new


def soap_bases(gradient, lstat, rstat, lbasis, rbasis, weights):
    count = gradient.shape[0]
    weights, gradient, lstat, rstat, lbasis, rbasis = lax.optimization_barrier(
        (weights, gradient, lstat, rstat, lbasis, rbasis)
    )
    lstat_new = stat_decay * lstat + (1.0 - stat_decay) * product(
        "nik,njk->nij", gradient, gradient
    )
    rstat_new = stat_decay * rstat + (1.0 - stat_decay) * product(
        "nki,nkj->nij", gradient, gradient
    )
    pending = product(
        "nij,njk->nik",
        jnp.concatenate([lstat_new, rstat_new], axis=0),
        jnp.concatenate([lbasis, rbasis], axis=0),
    )
    bases = orthogonal(pending)
    return weights, lstat_new, rstat_new, bases[:count], bases[count:]


def body(
    grad_parts,
    owner,
    master,
    first_moment,
    second_moment,
    left_stat,
    right_stat,
    left_basis,
    right_basis,
):
    shards = lax.axis_size("shard")
    groups = lax.axis_size("dp")
    my_group = lax.axis_index("dp")
    capacity = master.shape[2]
    block_size = master.shape[4]
    piece_len = grad_parts.shape[2]
    tile_count = owner.shape[0]
    per_group = tile_count // groups
    owners = owner.reshape(groups, per_group)
    place_index = owners * capacity + slot_index(owners, shards)
    own_place = lax.dynamic_index_in_dim(place_index, my_group, 0, keepdims=False)
    parts = grad_parts.reshape(groups, per_group, piece_len)
    summed = jnp.sum(lax.all_to_all(parts, "dp", 0, 0, tiled=True), axis=0)
    places = jnp.arange(capacity * shards, dtype=jnp.int32)
    placing = (places[:, None] == own_place[None, :]).astype(jnp.float32)
    outgoing = jnp.dot(placing, summed, precision=highest)
    outgoing = outgoing.reshape(shards, capacity, piece_len).transpose(1, 0, 2)
    incoming = lax.all_to_all(outgoing, "shard", split_axis=1, concat_axis=1, tiled=True)

    def as_tiles(array):
        return array.reshape(capacity, block_size, block_size)

    gradient = incoming.reshape(capacity, block_size, block_size)
    first_held = rotate(as_tiles(left_basis), as_tiles(first_moment), as_tiles(right_basis))
    master_held = as_tiles(master) * (1.0 - learn_rate * weight_decay)
    master_new, first_new, second_new = soap_weights(
        gradient,
        as_tiles(first_moment),
        as_tiles(second_moment),
        as_tiles(left_basis),
        as_tiles(right_basis),
        first_held,
        master_held,
    )
    weights = master_new.astype(jnp.bfloat16).transpose(1, 0, 2)
    weights, lstat_new, rstat_new, lbasis_new, rbasis_new = soap_bases(
        gradient,
        as_tiles(left_stat),
        as_tiles(right_stat),
        as_tiles(left_basis),
        as_tiles(right_basis),
        weights,
    )
    returned = lax.all_to_all(weights, "shard", split_axis=0, concat_axis=0, tiled=True)
    returned = returned.reshape(shards * capacity, piece_len)
    returned, lbasis_new, rbasis_new = lax.optimization_barrier((returned, lbasis_new, rbasis_new))
    picking = (own_place[:, None] == places[None, :]).astype(jnp.bfloat16)
    picking = jnp.broadcast_to(picking[None], (groups,) + picking.shape)
    spread = jnp.einsum("gtp,pc->gtc", picking, returned, preferred_element_type=jnp.float32)
    spread = spread.astype(jnp.bfloat16)
    new_params = lax.all_to_all(spread, "dp", 0, 0, tiled=True).reshape(tile_count, piece_len)
    results = (master_new, first_new, second_new, lstat_new, rstat_new, lbasis_new, rbasis_new)
    shaped = [item.reshape(1, 1, capacity, block_size, block_size) for item in results]
    return (new_params, *shaped)


def solution(mesh):
    state = P("dp", "shard", None, None, None)
    placed = (P("dp", None, "shard"), P()) + (state,) * 7
    return jax.shard_map(
        body,
        mesh=mesh,
        in_specs=placed,
        out_specs=(P(None, "shard"),) + (state,) * 7,
        check_vma=False,
    )
```

```python
import jax
import jax.numpy as jnp
from jax import lax
from jax.sharding import PartitionSpec as P

NS_STEPS = 10


beta_one = 0.9
beta_two = 0.95
stat_decay = 0.95
learn_rate = 0.05
weight_decay = 0.01
adam_eps = 1e-08
highest = lax.Precision.HIGHEST
high = lax.Precision.HIGH


def product(form, left, right, precision=high):
    return jnp.einsum(form, left, right, precision=precision)


def slot_index(owners, shards):
    matches = (owners[..., None] == jnp.arange(shards, dtype=jnp.int32)).astype(jnp.int32)
    running = jnp.cumsum(matches, axis=1)
    return jnp.sum(matches * running, axis=-1) - 1


def orthogonal(pending):
    iterate = pending * lax.rsqrt(jnp.sum(pending * pending, axis=(1, 2), keepdims=True) + 1e-06)
    def newton_schulz(step, iterate):
        gram = product("nik,njk->nij", iterate, iterate, high)
        return 1.5 * iterate - 0.5 * product("nij,njk->nik", gram, iterate, high)

    return lax.fori_loop(0, NS_STEPS, newton_schulz, iterate)


def soap_weights(gradient, master, first, second, lbasis, rbasis):
    count = gradient.shape[0]
    first_new = beta_one * first + (1.0 - beta_one) * gradient
    both = jnp.concatenate([gradient, first_new], axis=0)
    lboth = jnp.concatenate([lbasis, lbasis], axis=0)
    rboth = jnp.concatenate([rbasis, rbasis], axis=0)
    rotated = product("nik,nkl->nil", product("nji,njk->nik", lboth, both), rboth)
    grad_rot, first_rot = rotated[:count], rotated[count:]
    second_new = beta_two * second + (1.0 - beta_two) * grad_rot * grad_rot
    normed = first_rot / (jnp.sqrt(second_new) + adam_eps)
    update = product("nik,nlk->nil", product("nij,njk->nik", lbasis, normed), rbasis)
    master_new = master - learn_rate * (update + weight_decay * master)
    return master_new, first_new, second_new


def soap_bases(gradient, lstat, rstat, lbasis, rbasis, trips):
    count = gradient.shape[0]

    def refresh(carry):
        lstat_new = stat_decay * lstat + (1.0 - stat_decay) * product(
            "nik,njk->nij", gradient, gradient
        )
        rstat_new = stat_decay * rstat + (1.0 - stat_decay) * product(
            "nki,nkj->nij", gradient, gradient
        )
        pending = product(
            "nij,njk->nik",
            jnp.concatenate([lstat_new, rstat_new], axis=0),
            jnp.concatenate([lbasis, rbasis], axis=0),
        )
        return carry[0] + 1, lstat_new, rstat_new, orthogonal(pending)

    empty = jnp.zeros_like(lstat)
    _, lstat_new, rstat_new, bases = lax.while_loop(
        lambda carry: carry[0] < trips,
        refresh,
        (jnp.int32(0), empty, empty, jnp.concatenate([empty, empty], axis=0)),
    )
    return lstat_new, rstat_new, bases[:count], bases[count:]


def body(
    grad_parts,
    owner,
    master,
    first_moment,
    second_moment,
    left_stat,
    right_stat,
    left_basis,
    right_basis,
):
    shards = lax.axis_size("shard")
    groups = lax.axis_size("dp")
    my_group = lax.axis_index("dp")
    capacity = master.shape[2]
    block_size = master.shape[4]
    piece_len = grad_parts.shape[2]
    tile_count = owner.shape[0]
    per_group = tile_count // groups
    owners = owner.reshape(groups, per_group)
    place_index = owners * capacity + slot_index(owners, shards)
    own_place = lax.dynamic_index_in_dim(place_index, my_group, 0, keepdims=False)
    parts = grad_parts.reshape(groups, per_group, piece_len)
    summed = jnp.sum(lax.all_to_all(parts, "dp", 0, 0, tiled=True), axis=0)
    places = jnp.arange(capacity * shards, dtype=jnp.int32)
    placing = (places[:, None] == own_place[None, :]).astype(jnp.float32)
    outgoing = jnp.dot(placing, summed, precision=highest)
    outgoing = outgoing.reshape(shards, capacity, piece_len).transpose(1, 0, 2)
    incoming = lax.all_to_all(outgoing, "shard", split_axis=1, concat_axis=1, tiled=True)

    def as_tiles(array):
        return array.reshape(capacity, block_size, block_size)

    gradient = incoming.reshape(capacity, block_size, block_size)
    master_new, first_new, second_new = soap_weights(
        gradient,
        as_tiles(master),
        as_tiles(first_moment),
        as_tiles(second_moment),
        as_tiles(left_basis),
        as_tiles(right_basis),
    )
    weights = master_new.astype(jnp.bfloat16)
    weights = weights.transpose(1, 0, 2)
    returned = lax.all_to_all(weights, "shard", split_axis=0, concat_axis=0, tiled=True)
    returned = returned.reshape(shards * capacity, piece_len)
    picking = (own_place[:, None] == places[None, :]).astype(jnp.bfloat16)
    picking = jnp.broadcast_to(picking[None], (groups,) + picking.shape)
    spread = jnp.einsum("gtp,pc->gtc", picking, returned, preferred_element_type=jnp.float32)
    spread = spread.astype(jnp.bfloat16)
    new_params = lax.all_to_all(spread, "dp", 0, 0, tiled=True).reshape(tile_count, piece_len)
    lstat_new, rstat_new, lbasis_new, rbasis_new = soap_bases(
        gradient,
        as_tiles(left_stat),
        as_tiles(right_stat),
        as_tiles(left_basis),
        as_tiles(right_basis),
        1 + jnp.minimum(my_group, 0),
    )
    results = (master_new, first_new, second_new, lstat_new, rstat_new, lbasis_new, rbasis_new)
    shaped = [item.reshape(1, 1, capacity, block_size, block_size) for item in results]
    return (new_params, *shaped)


def solution(mesh):
    state = P("dp", "shard", None, None, None)
    placed = (P("dp", None, "shard"), P()) + (state,) * 7
    return jax.shard_map(
        body,
        mesh=mesh,
        in_specs=placed,
        out_specs=(P(None, "shard"),) + (state,) * 7,
        check_vma=False,
    )
```

```python
import jax
import jax.numpy as jnp
from jax import lax
from jax.sharding import PartitionSpec as P

NS_STEPS = 10


beta_one = 0.9
beta_two = 0.95
stat_decay = 0.95
learn_rate = 0.05
weight_decay = 0.01
adam_eps = 1e-08
highest = lax.Precision.HIGHEST
high = lax.Precision.HIGH


def product(form, left, right, precision=high):
    return jnp.einsum(form, left, right, precision=precision)


def slot_index(owners, shards):
    matches = (owners[..., None] == jnp.arange(shards, dtype=jnp.int32)).astype(jnp.int32)
    running = jnp.cumsum(matches, axis=1)
    return jnp.sum(matches * running, axis=-1) - 1


def orthogonal(pending):
    iterate = pending * lax.rsqrt(jnp.sum(pending * pending, axis=(1, 2), keepdims=True) + 1e-06)
    def newton_schulz(step, iterate):
        gram = product("nik,njk->nij", iterate, iterate, high)
        return 1.5 * iterate - 0.5 * product("nij,njk->nik", gram, iterate, high)

    return lax.fori_loop(0, NS_STEPS, newton_schulz, iterate)


def soap_weights(gradient, master, first, second, lbasis, rbasis):
    count = gradient.shape[0]
    first_new = beta_one * first + (1.0 - beta_one) * gradient
    both = jnp.concatenate([gradient, first_new], axis=0)
    lboth = jnp.concatenate([lbasis, lbasis], axis=0)
    rboth = jnp.concatenate([rbasis, rbasis], axis=0)
    rotated = product("nik,nkl->nil", product("nji,njk->nik", lboth, both), rboth)
    grad_rot, first_rot = rotated[:count], rotated[count:]
    second_new = beta_two * second + (1.0 - beta_two) * grad_rot * grad_rot
    normed = first_rot / (jnp.sqrt(second_new) + adam_eps)
    update = product("nik,nlk->nil", product("nij,njk->nik", lbasis, normed), rbasis)
    master_new = master - learn_rate * (update + weight_decay * master)
    return master_new, first_new, second_new


def soap_bases(gradient, lstat, rstat, lbasis, rbasis, taken):
    count = gradient.shape[0]

    def refresh(gradient, lstat, rstat, lbasis, rbasis):
        lstat_new = stat_decay * lstat + (1.0 - stat_decay) * product(
            "nik,njk->nij", gradient, gradient
        )
        rstat_new = stat_decay * rstat + (1.0 - stat_decay) * product(
            "nki,nkj->nij", gradient, gradient
        )
        pending = product(
            "nij,njk->nik",
            jnp.concatenate([lstat_new, rstat_new], axis=0),
            jnp.concatenate([lbasis, rbasis], axis=0),
        )
        bases = orthogonal(pending)
        return lstat_new, rstat_new, bases[:count], bases[count:]

    def unused(gradient, lstat, rstat, lbasis, rbasis):
        return lstat, rstat, lbasis, rbasis

    return lax.cond(taken, refresh, unused, gradient, lstat, rstat, lbasis, rbasis)


def body(
    grad_parts,
    owner,
    master,
    first_moment,
    second_moment,
    left_stat,
    right_stat,
    left_basis,
    right_basis,
):
    shards = lax.axis_size("shard")
    groups = lax.axis_size("dp")
    my_group = lax.axis_index("dp")
    capacity = master.shape[2]
    block_size = master.shape[4]
    piece_len = grad_parts.shape[2]
    tile_count = owner.shape[0]
    per_group = tile_count // groups
    owners = owner.reshape(groups, per_group)
    place_index = owners * capacity + slot_index(owners, shards)
    own_place = lax.dynamic_index_in_dim(place_index, my_group, 0, keepdims=False)
    parts = grad_parts.reshape(groups, per_group, piece_len)
    summed = jnp.sum(lax.all_to_all(parts, "dp", 0, 0, tiled=True), axis=0)
    places = jnp.arange(capacity * shards, dtype=jnp.int32)
    placing = (places[:, None] == own_place[None, :]).astype(jnp.float32)
    outgoing = jnp.dot(placing, summed, precision=highest)
    outgoing = outgoing.reshape(shards, capacity, piece_len).transpose(1, 0, 2)
    incoming = lax.all_to_all(outgoing, "shard", split_axis=1, concat_axis=1, tiled=True)

    def as_tiles(array):
        return array.reshape(capacity, block_size, block_size)

    gradient = incoming.reshape(capacity, block_size, block_size)
    master_new, first_new, second_new = soap_weights(
        gradient,
        as_tiles(master),
        as_tiles(first_moment),
        as_tiles(second_moment),
        as_tiles(left_basis),
        as_tiles(right_basis),
    )
    weights = master_new.astype(jnp.bfloat16)
    weights = weights.transpose(1, 0, 2)
    returned = lax.all_to_all(weights, "shard", split_axis=0, concat_axis=0, tiled=True)
    returned = returned.reshape(shards * capacity, piece_len)
    picking = (own_place[:, None] == places[None, :]).astype(jnp.bfloat16)
    picking = jnp.broadcast_to(picking[None], (groups,) + picking.shape)
    spread = jnp.einsum("gtp,pc->gtc", picking, returned, preferred_element_type=jnp.float32)
    spread = spread.astype(jnp.bfloat16)
    new_params = lax.all_to_all(spread, "dp", 0, 0, tiled=True).reshape(tile_count, piece_len)
    lstat_new, rstat_new, lbasis_new, rbasis_new = soap_bases(
        gradient,
        as_tiles(left_stat),
        as_tiles(right_stat),
        as_tiles(left_basis),
        as_tiles(right_basis),
        my_group >= 0,
    )
    results = (master_new, first_new, second_new, lstat_new, rstat_new, lbasis_new, rbasis_new)
    shaped = [item.reshape(1, 1, capacity, block_size, block_size) for item in results]
    return (new_params, *shaped)


def solution(mesh):
    state = P("dp", "shard", None, None, None)
    placed = (P("dp", None, "shard"), P()) + (state,) * 7
    return jax.shard_map(
        body,
        mesh=mesh,
        in_specs=placed,
        out_specs=(P(None, "shard"),) + (state,) * 7,
        check_vma=False,
    )
```

```python
import jax
import jax.numpy as jnp
from jax import lax
from jax.sharding import PartitionSpec as P

NS_STEPS = 10


beta_one = 0.9
beta_two = 0.95
stat_decay = 0.95
learn_rate = 0.05
weight_decay = 0.01
adam_eps = 1e-08
highest = lax.Precision.HIGHEST
high = lax.Precision.HIGH


def product(form, left, right, precision=high):
    return jnp.einsum(form, left, right, precision=precision)


def slot_index(owners, shards):
    matches = (owners[..., None] == jnp.arange(shards, dtype=jnp.int32)).astype(jnp.int32)
    running = jnp.cumsum(matches, axis=1)
    return jnp.sum(matches * running, axis=-1) - 1


def normalized(pending):
    return pending * lax.rsqrt(jnp.sum(pending * pending, axis=(1, 2), keepdims=True) + 1e-06)


def newton_schulz(step, iterate):
    gram = product("nik,njk->nij", iterate, iterate, high)
    return 1.5 * iterate - 0.5 * product("nij,njk->nik", gram, iterate, high)


def soap_weights(gradient, master, first, second, lbasis, rbasis):
    count = gradient.shape[0]
    first_new = beta_one * first + (1.0 - beta_one) * gradient
    both = jnp.concatenate([gradient, first_new], axis=0)
    lboth = jnp.concatenate([lbasis, lbasis], axis=0)
    rboth = jnp.concatenate([rbasis, rbasis], axis=0)
    rotated = product("nik,nkl->nil", product("nji,njk->nik", lboth, both), rboth)
    grad_rot, first_rot = rotated[:count], rotated[count:]
    second_new = beta_two * second + (1.0 - beta_two) * grad_rot * grad_rot
    normed = first_rot / (jnp.sqrt(second_new) + adam_eps)
    update = product("nik,nlk->nil", product("nij,njk->nik", lbasis, normed), rbasis)
    master_new = master - learn_rate * (update + weight_decay * master)
    return master_new, first_new, second_new


def soap_bases(gradient, lstat, rstat, lbasis, rbasis, taken, early_steps):
    def refresh(gradient, lstat, rstat, lbasis, rbasis):
        lstat_new = stat_decay * lstat + (1.0 - stat_decay) * product(
            "nik,njk->nij", gradient, gradient
        )
        rstat_new = stat_decay * rstat + (1.0 - stat_decay) * product(
            "nki,nkj->nij", gradient, gradient
        )
        pending = product(
            "nij,njk->nik",
            jnp.concatenate([lstat_new, rstat_new], axis=0),
            jnp.concatenate([lbasis, rbasis], axis=0),
        )
        iterate = lax.fori_loop(0, early_steps, newton_schulz, normalized(pending))
        return lstat_new, rstat_new, iterate

    def unused(gradient, lstat, rstat, lbasis, rbasis):
        return lstat, rstat, jnp.concatenate([lbasis, rbasis], axis=0)

    return lax.cond(taken, refresh, unused, gradient, lstat, rstat, lbasis, rbasis)


def finish_bases(iterate, taken, early_steps):
    def rest(iterate):
        return lax.fori_loop(early_steps, NS_STEPS, newton_schulz, iterate)

    return lax.cond(taken, rest, lambda iterate: iterate, iterate)


def body(
    grad_parts,
    owner,
    master,
    first_moment,
    second_moment,
    left_stat,
    right_stat,
    left_basis,
    right_basis,
):
    shards = lax.axis_size("shard")
    groups = lax.axis_size("dp")
    my_group = lax.axis_index("dp")
    capacity = master.shape[2]
    block_size = master.shape[4]
    piece_len = grad_parts.shape[2]
    tile_count = owner.shape[0]
    per_group = tile_count // groups
    owners = owner.reshape(groups, per_group)
    place_index = owners * capacity + slot_index(owners, shards)
    own_place = lax.dynamic_index_in_dim(place_index, my_group, 0, keepdims=False)
    parts = grad_parts.reshape(groups, per_group, piece_len)
    summed = jnp.sum(lax.all_to_all(parts, "dp", 0, 0, tiled=True), axis=0)
    places = jnp.arange(capacity * shards, dtype=jnp.int32)
    placing = (places[:, None] == own_place[None, :]).astype(jnp.float32)
    outgoing = jnp.dot(placing, summed, precision=highest)
    outgoing = outgoing.reshape(shards, capacity, piece_len).transpose(1, 0, 2)
    incoming = lax.all_to_all(outgoing, "shard", split_axis=1, concat_axis=1, tiled=True)

    def as_tiles(array):
        return array.reshape(capacity, block_size, block_size)

    gradient = incoming.reshape(capacity, block_size, block_size)
    master_new, first_new, second_new = soap_weights(
        gradient,
        as_tiles(master),
        as_tiles(first_moment),
        as_tiles(second_moment),
        as_tiles(left_basis),
        as_tiles(right_basis),
    )
    weights = master_new.astype(jnp.bfloat16)
    weights = weights.transpose(1, 0, 2)
    taken = my_group >= 0
    early_steps = NS_STEPS - 2
    lstat_new, rstat_new, iterate = soap_bases(
        gradient,
        as_tiles(left_stat),
        as_tiles(right_stat),
        as_tiles(left_basis),
        as_tiles(right_basis),
        taken,
        early_steps,
    )
    returned = lax.all_to_all(weights, "shard", split_axis=0, concat_axis=0, tiled=True)
    returned = returned.reshape(shards * capacity, piece_len)
    returned, iterate = lax.optimization_barrier((returned, iterate))
    picking = (own_place[:, None] == places[None, :]).astype(jnp.bfloat16)
    picking = jnp.broadcast_to(picking[None], (groups,) + picking.shape)
    spread = jnp.einsum("gtp,pc->gtc", picking, returned, preferred_element_type=jnp.float32)
    spread = spread.astype(jnp.bfloat16)
    new_params = lax.all_to_all(spread, "dp", 0, 0, tiled=True).reshape(tile_count, piece_len)
    bases = finish_bases(iterate, taken, early_steps)
    lbasis_new, rbasis_new = bases[:capacity], bases[capacity:]
    results = (master_new, first_new, second_new, lstat_new, rstat_new, lbasis_new, rbasis_new)
    shaped = [item.reshape(1, 1, capacity, block_size, block_size) for item in results]
    return (new_params, *shaped)


def solution(mesh):
    state = P("dp", "shard", None, None, None)
    placed = (P("dp", None, "shard"), P()) + (state,) * 7
    return jax.shard_map(
        body,
        mesh=mesh,
        in_specs=placed,
        out_specs=(P(None, "shard"),) + (state,) * 7,
        check_vma=False,
    )
```

```python
import jax
import jax.numpy as jnp
from jax import lax
from jax.sharding import PartitionSpec as P

NS_STEPS = 10


beta_one = 0.9
beta_two = 0.95
stat_decay = 0.95
learn_rate = 0.05
weight_decay = 0.01
adam_eps = 1e-08
highest = lax.Precision.HIGHEST
high = lax.Precision.HIGH


def product(form, left, right, precision=high):
    return jnp.einsum(form, left, right, precision=precision)


def slot_index(owners, shards):
    matches = (owners[..., None] == jnp.arange(shards, dtype=jnp.int32)).astype(jnp.int32)
    running = jnp.cumsum(matches, axis=1)
    return jnp.sum(matches * running, axis=-1) - 1


def orthogonal(pending):
    iterate = pending * lax.rsqrt(jnp.sum(pending * pending, axis=(1, 2), keepdims=True) + 1e-06)
    def newton_schulz(step, iterate):
        gram = product("nik,njk->nij", iterate, iterate, high)
        return 1.5 * iterate - 0.5 * product("nij,njk->nik", gram, iterate, high)

    for step in range(NS_STEPS):
        iterate = newton_schulz(step, iterate)
    return iterate


def soap_weights(gradient, master, first, second, lbasis, rbasis):
    count = gradient.shape[0]
    first_new = beta_one * first + (1.0 - beta_one) * gradient
    both = jnp.concatenate([gradient, first_new], axis=0)
    lboth = jnp.concatenate([lbasis, lbasis], axis=0)
    rboth = jnp.concatenate([rbasis, rbasis], axis=0)
    rotated = product("nik,nkl->nil", product("nji,njk->nik", lboth, both), rboth)
    grad_rot, first_rot = rotated[:count], rotated[count:]
    second_new = beta_two * second + (1.0 - beta_two) * grad_rot * grad_rot
    normed = first_rot / (jnp.sqrt(second_new) + adam_eps)
    update = product("nik,nlk->nil", product("nij,njk->nik", lbasis, normed), rbasis)
    master_new = master - learn_rate * (update + weight_decay * master)
    return master_new, first_new, second_new


def soap_bases(gradient, lstat, rstat, lbasis, rbasis, taken):
    count = gradient.shape[0]

    def refresh(gradient, lstat, rstat, lbasis, rbasis):
        lstat_new = stat_decay * lstat + (1.0 - stat_decay) * product(
            "nik,njk->nij", gradient, gradient
        )
        rstat_new = stat_decay * rstat + (1.0 - stat_decay) * product(
            "nki,nkj->nij", gradient, gradient
        )
        pending = product(
            "nij,njk->nik",
            jnp.concatenate([lstat_new, rstat_new], axis=0),
            jnp.concatenate([lbasis, rbasis], axis=0),
        )
        bases = orthogonal(pending)
        return lstat_new, rstat_new, bases[:count], bases[count:]

    def unused(gradient, lstat, rstat, lbasis, rbasis):
        return lstat, rstat, lbasis, rbasis

    return lax.cond(taken, refresh, unused, gradient, lstat, rstat, lbasis, rbasis)


def body(
    grad_parts,
    owner,
    master,
    first_moment,
    second_moment,
    left_stat,
    right_stat,
    left_basis,
    right_basis,
):
    shards = lax.axis_size("shard")
    groups = lax.axis_size("dp")
    my_group = lax.axis_index("dp")
    capacity = master.shape[2]
    block_size = master.shape[4]
    piece_len = grad_parts.shape[2]
    tile_count = owner.shape[0]
    per_group = tile_count // groups
    owners = owner.reshape(groups, per_group)
    place_index = owners * capacity + slot_index(owners, shards)
    own_place = lax.dynamic_index_in_dim(place_index, my_group, 0, keepdims=False)
    parts = grad_parts.reshape(groups, per_group, piece_len)
    summed = jnp.sum(lax.all_to_all(parts, "dp", 0, 0, tiled=True), axis=0)
    places = jnp.arange(capacity * shards, dtype=jnp.int32)
    placing = (places[:, None] == own_place[None, :]).astype(jnp.float32)
    outgoing = jnp.dot(placing, summed, precision=highest)
    outgoing = outgoing.reshape(shards, capacity, piece_len).transpose(1, 0, 2)
    incoming = lax.all_to_all(outgoing, "shard", split_axis=1, concat_axis=1, tiled=True)

    def as_tiles(array):
        return array.reshape(capacity, block_size, block_size)

    gradient = incoming.reshape(capacity, block_size, block_size)
    master_new, first_new, second_new = soap_weights(
        gradient,
        as_tiles(master),
        as_tiles(first_moment),
        as_tiles(second_moment),
        as_tiles(left_basis),
        as_tiles(right_basis),
    )
    weights = master_new.astype(jnp.bfloat16)
    weights = weights.transpose(1, 0, 2)
    returned = lax.all_to_all(weights, "shard", split_axis=0, concat_axis=0, tiled=True)
    returned = returned.reshape(shards * capacity, piece_len)
    picking = (own_place[:, None] == places[None, :]).astype(jnp.bfloat16)
    picking = jnp.broadcast_to(picking[None], (groups,) + picking.shape)
    spread = jnp.einsum("gtp,pc->gtc", picking, returned, preferred_element_type=jnp.float32)
    spread = spread.astype(jnp.bfloat16)
    new_params = lax.all_to_all(spread, "dp", 0, 0, tiled=True).reshape(tile_count, piece_len)
    lstat_new, rstat_new, lbasis_new, rbasis_new = soap_bases(
        gradient,
        as_tiles(left_stat),
        as_tiles(right_stat),
        as_tiles(left_basis),
        as_tiles(right_basis),
        my_group >= 0,
    )
    results = (master_new, first_new, second_new, lstat_new, rstat_new, lbasis_new, rbasis_new)
    shaped = [item.reshape(1, 1, capacity, block_size, block_size) for item in results]
    return (new_params, *shaped)


def solution(mesh):
    state = P("dp", "shard", None, None, None)
    placed = (P("dp", None, "shard"), P()) + (state,) * 7
    return jax.shard_map(
        body,
        mesh=mesh,
        in_specs=placed,
        out_specs=(P(None, "shard"),) + (state,) * 7,
        check_vma=False,
    )
```

```python
import jax
import jax.numpy as jnp
from jax import lax
from jax.sharding import PartitionSpec as P

NS_STEPS = 10


beta_one = 0.9
beta_two = 0.95
stat_decay = 0.95
learn_rate = 0.05
weight_decay = 0.01
adam_eps = 1e-08
highest = lax.Precision.HIGHEST
high = lax.Precision.HIGH


def product(form, left, right, precision=high):
    return jnp.einsum(form, left, right, precision=precision)


def slot_index(owners, shards):
    matches = (owners[..., None] == jnp.arange(shards, dtype=jnp.int32)).astype(jnp.int32)
    running = jnp.cumsum(matches, axis=1)
    return jnp.sum(matches * running, axis=-1) - 1


def orthogonal(pending):
    iterate = pending * lax.rsqrt(jnp.sum(pending * pending, axis=(1, 2), keepdims=True) + 1e-06)
    def newton_schulz(step, iterate):
        gram = product("nki,nkj->nij", iterate, iterate, high)
        return 1.5 * iterate - 0.5 * product("nij,njk->nik", iterate, gram, high)

    for step in range(NS_STEPS):
        iterate = newton_schulz(step, iterate)
    return iterate


def soap_weights(gradient, master, first, second, lbasis, rbasis):
    count = gradient.shape[0]
    first_new = beta_one * first + (1.0 - beta_one) * gradient
    both = jnp.concatenate([gradient, first_new], axis=0)
    lboth = jnp.concatenate([lbasis, lbasis], axis=0)
    rboth = jnp.concatenate([rbasis, rbasis], axis=0)
    rotated = product("nik,nkl->nil", product("nji,njk->nik", lboth, both), rboth)
    grad_rot, first_rot = rotated[:count], rotated[count:]
    second_new = beta_two * second + (1.0 - beta_two) * grad_rot * grad_rot
    normed = first_rot / (jnp.sqrt(second_new) + adam_eps)
    update = product("nik,nlk->nil", product("nij,njk->nik", lbasis, normed), rbasis)
    master_new = master - learn_rate * (update + weight_decay * master)
    return master_new, first_new, second_new


def soap_bases(gradient, lstat, rstat, lbasis, rbasis, taken):
    count = gradient.shape[0]

    def refresh(gradient, lstat, rstat, lbasis, rbasis):
        lstat_new = stat_decay * lstat + (1.0 - stat_decay) * product(
            "nik,njk->nij", gradient, gradient
        )
        rstat_new = stat_decay * rstat + (1.0 - stat_decay) * product(
            "nki,nkj->nij", gradient, gradient
        )
        pending = product(
            "nij,njk->nik",
            jnp.concatenate([lstat_new, rstat_new], axis=0),
            jnp.concatenate([lbasis, rbasis], axis=0),
        )
        bases = orthogonal(pending)
        return lstat_new, rstat_new, bases[:count], bases[count:]

    def unused(gradient, lstat, rstat, lbasis, rbasis):
        return lstat, rstat, lbasis, rbasis

    return lax.cond(taken, refresh, unused, gradient, lstat, rstat, lbasis, rbasis)


def body(
    grad_parts,
    owner,
    master,
    first_moment,
    second_moment,
    left_stat,
    right_stat,
    left_basis,
    right_basis,
):
    shards = lax.axis_size("shard")
    groups = lax.axis_size("dp")
    my_group = lax.axis_index("dp")
    capacity = master.shape[2]
    block_size = master.shape[4]
    piece_len = grad_parts.shape[2]
    tile_count = owner.shape[0]
    per_group = tile_count // groups
    owners = owner.reshape(groups, per_group)
    place_index = owners * capacity + slot_index(owners, shards)
    own_place = lax.dynamic_index_in_dim(place_index, my_group, 0, keepdims=False)
    parts = grad_parts.reshape(groups, per_group, piece_len)
    summed = jnp.sum(lax.all_to_all(parts, "dp", 0, 0, tiled=True), axis=0)
    places = jnp.arange(capacity * shards, dtype=jnp.int32)
    placing = (places[:, None] == own_place[None, :]).astype(jnp.float32)
    outgoing = jnp.dot(placing, summed, precision=highest)
    outgoing = outgoing.reshape(shards, capacity, piece_len).transpose(1, 0, 2)
    incoming = lax.all_to_all(outgoing, "shard", split_axis=1, concat_axis=1, tiled=True)

    def as_tiles(array):
        return array.reshape(capacity, block_size, block_size)

    gradient = incoming.reshape(capacity, block_size, block_size)
    master_new, first_new, second_new = soap_weights(
        gradient,
        as_tiles(master),
        as_tiles(first_moment),
        as_tiles(second_moment),
        as_tiles(left_basis),
        as_tiles(right_basis),
    )
    weights = master_new.astype(jnp.bfloat16)
    weights = weights.transpose(1, 0, 2)
    returned = lax.all_to_all(weights, "shard", split_axis=0, concat_axis=0, tiled=True)
    returned = returned.reshape(shards * capacity, piece_len)
    picking = (own_place[:, None] == places[None, :]).astype(jnp.bfloat16)
    picking = jnp.broadcast_to(picking[None], (groups,) + picking.shape)
    spread = jnp.einsum("gtp,pc->gtc", picking, returned, preferred_element_type=jnp.float32)
    spread = spread.astype(jnp.bfloat16)
    new_params = lax.all_to_all(spread, "dp", 0, 0, tiled=True).reshape(tile_count, piece_len)
    lstat_new, rstat_new, lbasis_new, rbasis_new = soap_bases(
        gradient,
        as_tiles(left_stat),
        as_tiles(right_stat),
        as_tiles(left_basis),
        as_tiles(right_basis),
        my_group >= 0,
    )
    results = (master_new, first_new, second_new, lstat_new, rstat_new, lbasis_new, rbasis_new)
    shaped = [item.reshape(1, 1, capacity, block_size, block_size) for item in results]
    return (new_params, *shaped)


def solution(mesh):
    state = P("dp", "shard", None, None, None)
    placed = (P("dp", None, "shard"), P()) + (state,) * 7
    return jax.shard_map(
        body,
        mesh=mesh,
        in_specs=placed,
        out_specs=(P(None, "shard"),) + (state,) * 7,
        check_vma=False,
    )
```

```python
import jax
import jax.numpy as jnp
from jax import lax
from jax.sharding import PartitionSpec as P

NS_STEPS = 10


beta_one = 0.9
beta_two = 0.95
stat_decay = 0.95
learn_rate = 0.05
weight_decay = 0.01
adam_eps = 1e-08
highest = lax.Precision.HIGHEST
high = lax.Precision.HIGH


def product(form, left, right, precision=high):
    return jnp.einsum(form, left, right, precision=precision)


def slot_index(owners, shards):
    matches = (owners[..., None] == jnp.arange(shards, dtype=jnp.int32)).astype(jnp.int32)
    running = jnp.cumsum(matches, axis=1)
    return jnp.sum(matches * running, axis=-1) - 1


def orthogonal(pending):
    iterate = pending * lax.rsqrt(jnp.sum(pending * pending, axis=(1, 2), keepdims=True) + 1e-06)
    def newton_schulz(step, iterate):
        gram = product("nki,nkj->nij", iterate, iterate, high)
        return 1.5 * iterate - 0.5 * product("nij,njk->nik", iterate, gram, high)

    for step in range(NS_STEPS):
        iterate = newton_schulz(step, iterate)
    return iterate


def soap_weights(gradient, master, first, second, lbasis, rbasis):
    count = gradient.shape[0]
    first_new = beta_one * first + (1.0 - beta_one) * gradient
    both = jnp.concatenate([gradient, first_new], axis=0)
    lboth = jnp.concatenate([lbasis, lbasis], axis=0)
    rboth = jnp.concatenate([rbasis, rbasis], axis=0)
    rotated = product("nik,nkl->nil", product("nji,njk->nik", lboth, both), rboth)
    grad_rot, first_rot = rotated[:count], rotated[count:]
    second_new = beta_two * second + (1.0 - beta_two) * grad_rot * grad_rot
    normed = first_rot / (jnp.sqrt(second_new) + adam_eps)
    update = product("nik,nlk->nil", product("nij,njk->nik", lbasis, normed), rbasis)
    master_new = master - learn_rate * (update + weight_decay * master)
    return master_new, first_new, second_new


def soap_bases(gradient, lstat, rstat, lbasis, rbasis, taken):
    count = gradient.shape[0]

    def refresh(gradient, lstat, rstat, lbasis, rbasis):
        lstat_new = stat_decay * lstat + (1.0 - stat_decay) * product(
            "nik,njk->nij", gradient, gradient
        )
        rstat_new = stat_decay * rstat + (1.0 - stat_decay) * product(
            "nki,nkj->nij", gradient, gradient
        )
        pending = product(
            "nij,njk->nik",
            jnp.concatenate([lstat_new, rstat_new], axis=0),
            jnp.concatenate([lbasis, rbasis], axis=0),
        )
        bases = orthogonal(pending)
        return lstat_new, rstat_new, bases[:count], bases[count:]

    def unused(gradient, lstat, rstat, lbasis, rbasis):
        return lstat, rstat, lbasis, rbasis

    return lax.cond(taken, refresh, unused, gradient, lstat, rstat, lbasis, rbasis)


def body(
    grad_parts,
    owner,
    master,
    first_moment,
    second_moment,
    left_stat,
    right_stat,
    left_basis,
    right_basis,
):
    shards = lax.axis_size("shard")
    groups = lax.axis_size("dp")
    my_group = lax.axis_index("dp")
    capacity = master.shape[2]
    block_size = master.shape[4]
    piece_len = grad_parts.shape[2]
    tile_count = owner.shape[0]
    per_group = tile_count // groups
    owners = owner.reshape(groups, per_group)
    place_index = owners * capacity + slot_index(owners, shards)
    own_place = lax.dynamic_index_in_dim(place_index, my_group, 0, keepdims=False)
    parts = grad_parts.reshape(groups, per_group, piece_len)
    summed = jnp.sum(lax.all_to_all(parts, "dp", 0, 0, tiled=True), axis=0)
    places = jnp.arange(capacity * shards, dtype=jnp.int32)
    placing = (places[:, None] == own_place[None, :]).astype(jnp.float32)
    outgoing = jnp.dot(placing, summed, precision=highest)
    outgoing = outgoing.reshape(shards, capacity, piece_len).transpose(1, 0, 2)
    incoming = lax.all_to_all(outgoing, "shard", split_axis=1, concat_axis=1, tiled=True)

    def as_tiles(array):
        return array.reshape(capacity, block_size, block_size)

    gradient = incoming.reshape(capacity, block_size, block_size)
    master_new, first_new, second_new = soap_weights(
        gradient,
        as_tiles(master),
        as_tiles(first_moment),
        as_tiles(second_moment),
        as_tiles(left_basis),
        as_tiles(right_basis),
    )
    weights = master_new.astype(jnp.bfloat16)
    weights = weights.transpose(1, 0, 2)
    returned = lax.all_to_all(weights, "shard", split_axis=0, concat_axis=0, tiled=True)
    returned = returned.reshape(shards * capacity, piece_len)
    picking = (own_place[:, None] == places[None, :]).astype(jnp.bfloat16)
    picking = jnp.tile(picking, (groups, 1))
    spread = jnp.dot(picking, returned, preferred_element_type=jnp.float32)
    spread = spread.astype(jnp.bfloat16).reshape(groups, per_group, piece_len)
    new_params = lax.all_to_all(spread, "dp", 0, 0, tiled=True).reshape(tile_count, piece_len)
    lstat_new, rstat_new, lbasis_new, rbasis_new = soap_bases(
        gradient,
        as_tiles(left_stat),
        as_tiles(right_stat),
        as_tiles(left_basis),
        as_tiles(right_basis),
        my_group >= 0,
    )
    results = (master_new, first_new, second_new, lstat_new, rstat_new, lbasis_new, rbasis_new)
    shaped = [item.reshape(1, 1, capacity, block_size, block_size) for item in results]
    return (new_params, *shaped)


def solution(mesh):
    state = P("dp", "shard", None, None, None)
    placed = (P("dp", None, "shard"), P()) + (state,) * 7
    return jax.shard_map(
        body,
        mesh=mesh,
        in_specs=placed,
        out_specs=(P(None, "shard"),) + (state,) * 7,
        check_vma=False,
    )
```

```python
import jax
import jax.numpy as jnp
from jax import lax
from jax.sharding import PartitionSpec as P

NS_STEPS = 10


beta_one = 0.9
beta_two = 0.95
stat_decay = 0.95
learn_rate = 0.05
weight_decay = 0.01
adam_eps = 1e-08
highest = lax.Precision.HIGHEST
high = lax.Precision.HIGH


def product(form, left, right, precision=high):
    return jnp.einsum(form, left, right, precision=precision)


def slot_index(owners, shards):
    matches = (owners[..., None] == jnp.arange(shards, dtype=jnp.int32)).astype(jnp.int32)
    running = jnp.cumsum(matches, axis=1)
    return jnp.sum(matches * running, axis=-1) - 1


def orthogonal(pending):
    iterate = pending * lax.rsqrt(jnp.sum(pending * pending, axis=(1, 2), keepdims=True) + 1e-06)
    def newton_schulz(step, iterate):
        gram = product("nki,nkj->nij", iterate, iterate, high)
        return 1.5 * iterate - 0.5 * product("nij,njk->nik", iterate, gram, high)

    for step in range(NS_STEPS):
        iterate = newton_schulz(step, iterate)
    return iterate


def soap_weights(gradient, master, first, second, lbasis, rbasis):
    count = gradient.shape[0]
    first_new = beta_one * first + (1.0 - beta_one) * gradient
    both = jnp.concatenate([gradient, first_new], axis=0)
    lboth = jnp.concatenate([lbasis, lbasis], axis=0)
    rboth = jnp.concatenate([rbasis, rbasis], axis=0)
    rotated = product("nik,nkl->nil", product("nji,njk->nik", lboth, both), rboth)
    grad_rot, first_rot = rotated[:count], rotated[count:]
    second_new = beta_two * second + (1.0 - beta_two) * grad_rot * grad_rot
    normed = first_rot / (jnp.sqrt(second_new) + adam_eps)
    update = product("nij,njl->nil", lbasis, product("njk,nlk->njl", normed, rbasis))
    master_new = master - learn_rate * (update + weight_decay * master)
    return master_new, first_new, second_new


def soap_bases(gradient, lstat, rstat, lbasis, rbasis, taken):
    count = gradient.shape[0]

    def refresh(gradient, lstat, rstat, lbasis, rbasis):
        lstat_new = stat_decay * lstat + (1.0 - stat_decay) * product(
            "nik,njk->nij", gradient, gradient
        )
        rstat_new = stat_decay * rstat + (1.0 - stat_decay) * product(
            "nki,nkj->nij", gradient, gradient
        )
        pending = product(
            "nij,njk->nik",
            jnp.concatenate([lstat_new, rstat_new], axis=0),
            jnp.concatenate([lbasis, rbasis], axis=0),
        )
        bases = orthogonal(pending)
        return lstat_new, rstat_new, bases[:count], bases[count:]

    def unused(gradient, lstat, rstat, lbasis, rbasis):
        return lstat, rstat, lbasis, rbasis

    return lax.cond(taken, refresh, unused, gradient, lstat, rstat, lbasis, rbasis)


def body(
    grad_parts,
    owner,
    master,
    first_moment,
    second_moment,
    left_stat,
    right_stat,
    left_basis,
    right_basis,
):
    shards = lax.axis_size("shard")
    groups = lax.axis_size("dp")
    my_group = lax.axis_index("dp")
    capacity = master.shape[2]
    block_size = master.shape[4]
    piece_len = grad_parts.shape[2]
    tile_count = owner.shape[0]
    per_group = tile_count // groups
    owners = owner.reshape(groups, per_group)
    place_index = owners * capacity + slot_index(owners, shards)
    own_place = lax.dynamic_index_in_dim(place_index, my_group, 0, keepdims=False)
    parts = grad_parts.reshape(groups, per_group, piece_len)
    summed = jnp.sum(lax.all_to_all(parts, "dp", 0, 0, tiled=True), axis=0)
    places = jnp.arange(capacity * shards, dtype=jnp.int32)
    placing = (places[:, None] == own_place[None, :]).astype(jnp.float32)
    outgoing = jnp.dot(placing, summed, precision=highest)
    outgoing = outgoing.reshape(shards, capacity, piece_len).transpose(1, 0, 2)
    incoming = lax.all_to_all(outgoing, "shard", split_axis=1, concat_axis=1, tiled=True)

    def as_tiles(array):
        return array.reshape(capacity, block_size, block_size)

    gradient = incoming.reshape(capacity, block_size, block_size)
    master_new, first_new, second_new = soap_weights(
        gradient,
        as_tiles(master),
        as_tiles(first_moment),
        as_tiles(second_moment),
        as_tiles(left_basis),
        as_tiles(right_basis),
    )
    weights = master_new.astype(jnp.bfloat16)
    weights = weights.transpose(1, 0, 2)
    returned = lax.all_to_all(weights, "shard", split_axis=0, concat_axis=0, tiled=True)
    returned = returned.reshape(shards * capacity, piece_len)
    picking = (own_place[:, None] == places[None, :]).astype(jnp.bfloat16)
    picking = jnp.broadcast_to(picking[None], (groups,) + picking.shape)
    spread = jnp.einsum("gtp,pc->gtc", picking, returned, preferred_element_type=jnp.float32)
    spread = spread.astype(jnp.bfloat16)
    new_params = lax.all_to_all(spread, "dp", 0, 0, tiled=True).reshape(tile_count, piece_len)
    lstat_new, rstat_new, lbasis_new, rbasis_new = soap_bases(
        gradient,
        as_tiles(left_stat),
        as_tiles(right_stat),
        as_tiles(left_basis),
        as_tiles(right_basis),
        my_group >= 0,
    )
    results = (master_new, first_new, second_new, lstat_new, rstat_new, lbasis_new, rbasis_new)
    shaped = [item.reshape(1, 1, capacity, block_size, block_size) for item in results]
    return (new_params, *shaped)


def solution(mesh):
    state = P("dp", "shard", None, None, None)
    placed = (P("dp", None, "shard"), P()) + (state,) * 7
    return jax.shard_map(
        body,
        mesh=mesh,
        in_specs=placed,
        out_specs=(P(None, "shard"),) + (state,) * 7,
        check_vma=False,
    )
```
